256 devices in a mesh: seq: 64 (over y, z, core), head: 4 (over x).
Axes of the slice: x: 4, y: 4, z: 8, core: 2. Of those that a mesh axis runs over, the one named last changes fastest.
Arguments:
- queries: bfloat16 [32768, 4096], P(('seq', 'head')), may hold values from -6 to 6
- keys: bfloat16 [32768, 4096], P(('seq', 'head')), may hold values from -6 to 6
- values: bfloat16 [32768, 4096], P(('seq', 'head')), may hold values from -6 to 6
- cluster_ids: int32 [32, 32768, 1], P(None, 'seq'), may hold values from 0 to 127; in each aligned block of 128 rows (0 to 127, 128 to 255, ..., all dimensions but the last counted through in order) at most 2 rows name the same one
- out_weight: bfloat16 [4096, 4096], P('head', 'seq'), may hold values from -0.09375 to 0.09375
Outputs:
- projected: bfloat16 [32768, 4096], P('seq', 'head')
The draws below stay inside these ranges and needn't reach their ends.
Inputs may be any that keep to these rules, and one draw needn't show every extreme that they name: `cluster_ids`: in each aligned block of 128 tokens of one head (the rows of one device), no cluster id appears more than 2 times, and some cluster appears exactly 2 times.
All inputs are finite; a program needn't handle non-finite values.
Results may differ from the reference program's by a relative error of at most 0.014.
Values may be sent and summed in bfloat16 or wider, within the bound.
No kernel may reach another device: no remote copies, remote signals or barrier semaphores. Data moves between devices by JAX's collectives and lax.ppermute only.
A program may use at most 128 MiB of HBM per device.

```python
import math
import jax
import jax.numpy as jnp
import numpy as np
from jax import lax

D = 4096
HEADS = 32
HD = 128
CLUSTERS = 128
TOKENS = 32768
SUB = 128
MOST = 2
CAP = 512


def draw_queries(key, part):
    subkey = jax.random.fold_in(key, 101)
    return jnp.clip(jax.random.normal(subkey, (TOKENS, D), jnp.float32), -4.0, 4.0).astype(jnp.bfloat16)


def draw_keys(key, part):
    subkey = jax.random.fold_in(key, 202)
    return jnp.clip(jax.random.normal(subkey, (TOKENS, D), jnp.float32), -4.0, 4.0).astype(jnp.bfloat16)


def shard_levels(own_key, extent, split, low, largest):
    level, own = 1.0, jax.random.fold_in(own_key, 6)
    for dim, parts in split:
        steps = jnp.exp(jax.random.uniform(jax.random.fold_in(own, dim), (parts,), jnp.float32, low / len(split), largest / len(split)))
        level = level * jnp.repeat(steps, extent[dim] // parts).reshape([-1 if axis == dim else 1 for axis in range(len(extent))])
    return level


def shared_out(stream_key, own, number, rows, number_of, top, bound, skew):
    order = jax.random.permutation(stream_key, number_of)
    heavy_load, usual = portions_of(number_of, rows * top, bound, skew, True), portions_of(number_of, rows * top, bound, skew, False)
    places = jnp.arange(number_of)

    def named(tallies, rotation):
        used = int((tallies > 0).sum())
        fixed = max(1, used // 4)
        shifted = fixed + (places - fixed + rotation * (used - fixed)) % max(1, number_of - fixed)
        return jnp.zeros((number_of,), jnp.int32).at[order[jnp.where(places < fixed, places, shifted)]].set(jnp.asarray(tallies, jnp.int32))

    tallies = jnp.where(number % 4 == 0, named(heavy_load, number // 4), named(usual, number - number // 4 - 1))
    mixed = jax.random.permutation(jax.random.fold_in(own, 3), number_of)
    giver, sink = mixed[0:number_of // 2 * 2:2], mixed[1:number_of // 2 * 2:2]
    room = jnp.minimum(tallies[giver] - 1, bound - tallies[sink]) // 2
    room = jnp.where((giver == order[0]) | (sink == order[0]) | (tallies[sink] == 0), 0, jnp.maximum(room, 0))
    shifted = jax.random.randint(jax.random.fold_in(own, 4), (number_of // 2,), 0, 1 << 20) % (room + 1)
    tallies = tallies.at[giver].add(-shifted).at[sink].add(shifted)
    labels = jnp.searchsorted(jnp.cumsum(tallies), jnp.arange(rows * top), side="right").astype(jnp.int32)
    grid = labels.reshape(top, rows).T
    grid = grid[jax.random.permutation(jax.random.fold_in(own, 1), rows)]
    rotation = jax.random.randint(jax.random.fold_in(own, 2), (rows, 1), 0, top)
    return jnp.take_along_axis(grid, (jnp.arange(top)[None, :] + rotation) % top, axis=1)


def portions_of(count, total, most, slope, full):
    weights = [(1 << 20) // math.isqrt(rank ** slope) + 1 for rank in range(1, count + 1)]
    largest = most if full else min(most, max(-(-total // count), total * weights[0] // sum(weights)))
    least = 1 if total - largest >= count - 1 else 0
    given, rest = [largest] + [least] * (count - 1), total - largest - least * (count - 1)
    while rest > 0:
        candidates = [i for i in range(1, count) if given[i] < largest] or [i for i in range(1, count) if given[i] < most]
        whole, remaining = sum([weights[i] for i in candidates]), rest
        for i in candidates:
            more = min(most - given[i], max(1, remaining * weights[i] // whole), rest)
            given[i] = given[i] + more
            rest = rest - more
    return np.array(given)


def centred(stream_key, dims, deviation, bound, shards=(), kind=jnp.bfloat16):
    values = jax.random.normal(stream_key, dims, jnp.float32) * deviation
    if len(shards) > 0:
        values = shard_levels(stream_key, dims, shards, -0.22, 0.18) * values
    return jnp.clip(values, min=-bound, max=bound).astype(kind)


def setup_inputs(seed: int = 0) -> dict:
    splits = jax.random.split(jax.random.key(seed), 6)
    queries = draw_queries(jax.random.fold_in(splits[5], 71), 0)
    keys = draw_keys(jax.random.fold_in(splits[5], 71), 0)
    values = centred(splits[2], (TOKENS, D), 1.0, 6.0, ((0, 256),))
    cluster_ids_keys = jax.random.split(jax.random.fold_in(splits[3], 1), HEADS * TOKENS // SUB)
    cluster_ids_turns = jax.random.permutation(jax.random.fold_in(splits[3], 3), HEADS * TOKENS // SUB)
    cluster_ids = jax.vmap(lambda own, number: shared_out(jax.random.fold_in(splits[3], 2), own, number, SUB, CLUSTERS, 1, MOST, 2))(cluster_ids_keys, cluster_ids_turns).reshape((HEADS, TOKENS, 1))
    out_weight = centred(splits[4], (D, D), D ** -0.5, 0.09375, ((0, 4), (1, 64)))
    return dict(queries=queries, keys=keys, values=values, cluster_ids=cluster_ids, out_weight=out_weight)


def attend_head(inputs):
    query_head, key_head, value_head, head_ids = inputs
    cluster_range = jnp.arange(CLUSTERS, dtype=jnp.int32)
    counts = jnp.sum((head_ids[None, :] == cluster_range[:, None]).astype(jnp.int32), axis=1).astype(jnp.int32)
    starts = (jnp.cumsum(counts) - counts).astype(jnp.int32)
    ordering = jnp.argsort(head_ids, stable=True).astype(jnp.int32)
    sorted_ids = head_ids[ordering]
    position = jnp.arange(TOKENS, dtype=jnp.int32) - starts[sorted_ids]
    target = (sorted_ids * CAP + position).astype(jnp.int32)

    def place_rows(tensor):
        filled = jnp.zeros((CLUSTERS * CAP, HD), tensor.dtype).at[target].set(tensor[ordering])
        return filled.reshape(CLUSTERS, CAP, HD)

    query_block = place_rows(query_head)
    key_block = place_rows(key_head)
    value_block = place_rows(value_head)
    validity = jnp.arange(CAP, dtype=jnp.int32)[None, :] < counts[:, None]
    scores = jnp.einsum('cqd,ckd->cqk', query_block.astype(jnp.float32), key_block.astype(jnp.float32)) * (HD ** -0.5)
    scores = jnp.where(validity[:, None, :], scores, -1.0e30)
    row_max = jnp.max(scores, axis=-1, keepdims=True)
    raised = jnp.exp(scores - row_max)
    weights = (raised / jnp.sum(raised, axis=-1, keepdims=True)).astype(jnp.bfloat16)
    out_block = jnp.einsum('cqk,ckd->cqd', weights.astype(jnp.float32), value_block.astype(jnp.float32)).astype(jnp.bfloat16)
    flat_rows = out_block.reshape(CLUSTERS * CAP, HD)[target]
    return jnp.zeros((TOKENS, HD), jnp.bfloat16).at[ordering].set(flat_rows)


def split_heads(tensor):
    return tensor.reshape(TOKENS, HEADS, HD).transpose(1, 0, 2)


def reference(queries, keys, values, cluster_ids, out_weight):
    per_head = lax.map(attend_head, (split_heads(queries), split_heads(keys), split_heads(values), cluster_ids[:, :, 0]))
    attended = per_head.transpose(1, 0, 2).reshape(TOKENS, D)
    return jnp.dot(attended, out_weight, preferred_element_type=jnp.float32).astype(jnp.bfloat16)
```

```python
import jax
import jax.numpy as jnp
from jax import lax
from jax.sharding import PartitionSpec as P

HEADS = 32
HD = 128
CLUSTERS = 128


def slot_table(block_ids, slot_depth):
    sub_rows = block_ids.shape[-1]
    onehot = (block_ids[..., None] == jnp.arange(CLUSTERS, dtype=jnp.int32)).astype(jnp.float32)
    lower = (jnp.arange(sub_rows)[:, None] >= jnp.arange(sub_rows)[None, :]).astype(jnp.float32)
    running = jnp.einsum("ts,abse->abte", lower, onehot)
    ranking = (jnp.sum(running * onehot, axis=-1) - 1.0).astype(jnp.int32)
    depth_hit = (ranking[..., None] == jnp.arange(slot_depth, dtype=jnp.int32)).astype(jnp.bfloat16)
    return onehot.astype(jnp.bfloat16)[..., :, None] * depth_hit[..., None, :]


def attend_blocks(packed, validity):
    scores = jnp.einsum(
        "cqd,ckd->cqk", packed[0], packed[1], preferred_element_type=jnp.float32
    ) * HD ** (-0.5)
    scores = jnp.where(validity[:, None, :] > 0, scores, -1e30)
    row_max = jnp.max(scores, axis=-1, keepdims=True)
    raised = jnp.exp(scores - row_max)
    weights = (raised / jnp.sum(raised, axis=-1, keepdims=True)).astype(jnp.bfloat16)
    return jnp.einsum(
        "cqk,ckd->cqd", weights, packed[2], preferred_element_type=jnp.float32
    ).astype(jnp.bfloat16)


def body(queries, keys, values, cluster_ids, out_weight):
    n_seq = lax.axis_size("seq")
    n_head = lax.axis_size("head")
    head_group = lax.axis_index("head")
    tok_dev = cluster_ids.shape[1]
    sub_rows = tok_dev // n_head
    group_heads = HEADS // n_head
    slot_depth = max(2, 2 * tok_dev // (n_head * CLUSTERS))
    per_owner = group_heads * CLUSTERS // n_seq
    n_src = n_seq * n_head
    all_ids = cluster_ids[:, :, 0]

    own_ids = lax.dynamic_slice_in_dim(all_ids, head_group * sub_rows, sub_rows, 1)
    own_table = slot_table(own_ids[:, None, :], slot_depth)[:, 0]
    stacked = jnp.stack([t.reshape(sub_rows, HEADS, HD) for t in (queries, keys, values)])
    packed = jnp.einsum(
        "htcr,xthd->xhcrd", own_table, stacked, preferred_element_type=jnp.float32
    ).astype(jnp.bfloat16)
    packed = packed.reshape(3, n_head, per_owner, n_seq, slot_depth, HD)
    packed = packed.transpose(0, 3, 1, 2, 4, 5).reshape(3, n_src, per_owner, slot_depth, HD)
    markers = jnp.sum(own_table.astype(jnp.float32), axis=1).astype(jnp.bfloat16)
    markers = markers.reshape(n_head, per_owner, n_seq, slot_depth)
    markers = markers.transpose(2, 0, 1, 3).reshape(n_src, per_owner, slot_depth)

    arrived = lax.all_to_all(packed, ("seq", "head"), split_axis=1, concat_axis=1, tiled=True)
    valid = lax.all_to_all(markers, ("seq", "head"), split_axis=0, concat_axis=0, tiled=True)
    arrived = arrived.transpose(0, 2, 1, 3, 4).reshape(3, per_owner, n_src * slot_depth, HD)
    valid = valid.transpose(1, 0, 2).reshape(per_owner, n_src * slot_depth)
    result_block = attend_blocks(arrived, valid)
    result_block = result_block.reshape(per_owner, n_seq, n_head * slot_depth, HD)
    returned = lax.all_to_all(result_block, "seq", split_axis=1, concat_axis=1, tiled=True)
    returned = returned.reshape(group_heads, CLUSTERS, n_head, slot_depth, HD)

    group_ids = lax.dynamic_slice_in_dim(all_ids, head_group * group_heads, group_heads, 0)
    group_ids = group_ids.reshape(group_heads, n_head, sub_rows)
    home_table = slot_table(group_ids, slot_depth)
    gathered = jnp.einsum(
        "hltcr,hclrd->lthd", home_table, returned, preferred_element_type=jnp.float32
    ).astype(jnp.bfloat16)
    gathered = gathered.reshape(tok_dev, group_heads * HD)
    partial_value = jnp.dot(
        gathered,
        lax.all_gather(out_weight, "seq", axis=1, tiled=True),
        preferred_element_type=jnp.float32,
    )
    return lax.psum_scatter(
        partial_value.astype(jnp.bfloat16), "head", scatter_dimension=1, tiled=True
    )


def solution(mesh):
    in_specs = (
        P(("seq", "head"), None),
        P(("seq", "head"), None),
        P(("seq", "head"), None),
        P(None, "seq", None),
        P("head", "seq"),
    )
    out_specs = P("seq", "head")
    return jax.shard_map(body, mesh=mesh, in_specs=in_specs, out_specs=out_specs, check_vma=False)
```

```python
import jax
import jax.numpy as jnp
from jax import lax
from jax.sharding import PartitionSpec as P

HEADS = 32
HD = 128
CLUSTERS = 128


def slot_table(block_ids, slot_depth):
    sub_rows = block_ids.shape[-1]
    onehot = (block_ids[..., None] == jnp.arange(CLUSTERS, dtype=jnp.int32)).astype(jnp.float32)
    lower = (jnp.arange(sub_rows)[:, None] >= jnp.arange(sub_rows)[None, :]).astype(jnp.float32)
    running = jnp.einsum("ts,abse->abte", lower, onehot)
    ranking = (jnp.sum(running * onehot, axis=-1) - 1.0).astype(jnp.int32)
    depth_hit = (ranking[..., None] == jnp.arange(slot_depth, dtype=jnp.int32)).astype(jnp.bfloat16)
    return onehot.astype(jnp.bfloat16)[..., :, None] * depth_hit[..., None, :]


def attend_blocks(packed):
    validity = jnp.isfinite(packed[1][..., 0])
    keys = jnp.where(validity[..., None], packed[1], jnp.zeros_like(packed[1]))
    scores = jnp.einsum(
        "cqd,ckd->cqk", packed[0], keys, preferred_element_type=jnp.float32
    ) * HD ** (-0.5)
    scores = jnp.where(validity[:, None, :], scores, -1e30)
    row_max = jnp.max(scores, axis=-1, keepdims=True)
    raised = jnp.exp(scores - row_max)
    weights = (raised / jnp.sum(raised, axis=-1, keepdims=True)).astype(jnp.bfloat16)
    return jnp.einsum(
        "cqk,ckd->cqd", weights, packed[2], preferred_element_type=jnp.float32
    ).astype(jnp.bfloat16)


def body(queries, keys, values, cluster_ids, out_weight):
    n_seq = lax.axis_size("seq")
    n_head = lax.axis_size("head")
    head_group = lax.axis_index("head")
    tok_dev = cluster_ids.shape[1]
    sub_rows = tok_dev // n_head
    group_heads = HEADS // n_head
    slot_depth = max(2, 2 * tok_dev // (n_head * CLUSTERS))
    per_owner = group_heads * CLUSTERS // n_seq
    n_src = n_seq * n_head
    all_ids = cluster_ids[:, :, 0]

    own_ids = lax.dynamic_slice_in_dim(all_ids, head_group * sub_rows, sub_rows, 1)
    own_table = slot_table(own_ids[:, None, :], slot_depth)[:, 0]
    stacked = jnp.stack([t.reshape(sub_rows, HEADS, HD) for t in (queries, keys, values)])
    packed = jnp.einsum(
        "htcr,xthd->xhcrd", own_table, stacked, preferred_element_type=jnp.float32
    ).astype(jnp.bfloat16)
    packed = packed.reshape(3, n_head, per_owner, n_seq, slot_depth, HD)
    packed = packed.transpose(0, 3, 1, 2, 4, 5).reshape(3, n_src, per_owner, slot_depth, HD)
    filled = jnp.sum(own_table.astype(jnp.float32), axis=1)
    filled = filled.reshape(n_head, per_owner, n_seq, slot_depth).transpose(2, 0, 1, 3)
    filled = filled.reshape(n_src, per_owner, slot_depth, 1)
    packed = jnp.concatenate(
        [packed[:1], jnp.where(filled > 0, packed[1:2], jnp.inf).astype(jnp.bfloat16), packed[2:]]
    )

    arrived = lax.all_to_all(packed, ("seq", "head"), split_axis=1, concat_axis=1, tiled=True)
    arrived = arrived.transpose(0, 2, 1, 3, 4).reshape(3, per_owner, n_src * slot_depth, HD)
    result_block = attend_blocks(arrived)
    result_block = result_block.reshape(per_owner, n_seq, n_head * slot_depth, HD)
    returned = lax.all_to_all(result_block, "seq", split_axis=1, concat_axis=1, tiled=True)
    returned = returned.reshape(group_heads, CLUSTERS, n_head, slot_depth, HD)

    group_ids = lax.dynamic_slice_in_dim(all_ids, head_group * group_heads, group_heads, 0)
    group_ids = group_ids.reshape(group_heads, n_head, sub_rows)
    home_table = slot_table(group_ids, slot_depth)
    gathered = jnp.einsum(
        "hltcr,hclrd->lthd", home_table, returned, preferred_element_type=jnp.float32
    ).astype(jnp.bfloat16)
    gathered = gathered.reshape(tok_dev, group_heads * HD)
    partial_value = jnp.dot(
        gathered,
        lax.all_gather(out_weight, "seq", axis=1, tiled=True),
        preferred_element_type=jnp.float32,
    )
    return lax.psum_scatter(
        partial_value.astype(jnp.bfloat16), "head", scatter_dimension=1, tiled=True
    )


def solution(mesh):
    in_specs = (
        P(("seq", "head"), None),
        P(("seq", "head"), None),
        P(("seq", "head"), None),
        P(None, "seq", None),
        P("head", "seq"),
    )
    out_specs = P("seq", "head")
    return jax.shard_map(body, mesh=mesh, in_specs=in_specs, out_specs=out_specs, check_vma=False)
```

```python
import jax
import jax.numpy as jnp
from jax import lax
from jax.sharding import PartitionSpec as P

HEADS = 32
HD = 128
CLUSTERS = 128


def slot_table(block_ids, slot_depth):
    sub_rows = block_ids.shape[-1]
    onehot = (block_ids[..., None] == jnp.arange(CLUSTERS, dtype=jnp.int32)).astype(jnp.float32)
    lower = (jnp.arange(sub_rows)[:, None] >= jnp.arange(sub_rows)[None, :]).astype(jnp.float32)
    running = jnp.einsum("ts,abse->abte", lower, onehot)
    ranking = (jnp.sum(running * onehot, axis=-1) - 1.0).astype(jnp.int32)
    depth_hit = (ranking[..., None] == jnp.arange(slot_depth, dtype=jnp.int32)).astype(jnp.bfloat16)
    return onehot.astype(jnp.bfloat16)[..., :, None] * depth_hit[..., None, :]


def attend_blocks(packed, validity):
    scores = jnp.einsum(
        "cqd,ckd->cqk", packed[0], packed[1], preferred_element_type=jnp.float32
    ) * HD ** (-0.5)
    scores = jnp.where(validity[:, None, :] > 0, scores, -1e30)
    row_max = jnp.max(scores, axis=-1, keepdims=True)
    raised = jnp.exp(scores - row_max)
    weights = (raised / jnp.sum(raised, axis=-1, keepdims=True)).astype(jnp.bfloat16)
    return jnp.einsum(
        "cqk,ckd->cqd", weights, packed[2], preferred_element_type=jnp.float32
    ).astype(jnp.bfloat16)


def body(queries, keys, values, cluster_ids, out_weight):
    n_seq = lax.axis_size("seq")
    n_head = lax.axis_size("head")
    head_group = lax.axis_index("head")
    tok_dev = cluster_ids.shape[1]
    sub_rows = tok_dev // n_head
    group_heads = HEADS // n_head
    slot_depth = max(2, 2 * tok_dev // (n_head * CLUSTERS))
    per_owner = group_heads * CLUSTERS // n_seq
    n_src = n_seq * n_head
    all_ids = cluster_ids[:, :, 0]

    own_ids = lax.dynamic_slice_in_dim(all_ids, head_group * sub_rows, sub_rows, 1)
    own_table = slot_table(own_ids[:, None, :], slot_depth)[:, 0]
    stacked = jnp.stack([t.reshape(sub_rows, HEADS, HD) for t in (queries, keys, values)])
    packed = jnp.einsum(
        "htcr,xthd->xhcrd", own_table, stacked, preferred_element_type=jnp.float32
    ).astype(jnp.bfloat16)
    packed = packed.reshape(3, n_head, per_owner, n_seq, slot_depth, HD)
    packed = packed.transpose(0, 3, 1, 2, 4, 5).reshape(3, n_src, per_owner, slot_depth, HD)
    markers = jnp.sum(own_table.astype(jnp.float32), axis=1).astype(jnp.bfloat16)
    markers = markers.reshape(n_head, per_owner, n_seq, slot_depth)
    markers = markers.transpose(2, 0, 1, 3).reshape(n_src, per_owner, slot_depth)

    arrived = lax.all_to_all(packed, ("seq", "head"), split_axis=1, concat_axis=1, tiled=True)
    valid = lax.all_to_all(markers, ("seq", "head"), split_axis=0, concat_axis=0, tiled=True)
    arrived = arrived.transpose(0, 2, 1, 3, 4).reshape(3, per_owner, n_src * slot_depth, HD)
    valid = valid.transpose(1, 0, 2).reshape(per_owner, n_src * slot_depth)
    group_ids = lax.dynamic_slice_in_dim(all_ids, head_group * group_heads, group_heads, 0)
    group_ids = group_ids.reshape(group_heads, n_head, sub_rows)
    home_table = slot_table(group_ids, slot_depth)
    weight = lax.all_gather(out_weight, "seq", axis=1, tiled=True)

    halves = 2
    part_items = per_owner // halves
    part_heads = group_heads // halves
    projected = []
    for half in range(halves):
        items = slice(half * part_items, (half + 1) * part_items)
        result_block = attend_blocks(arrived[:, items], valid[items])
        result_block = result_block.reshape(part_items, n_seq, n_head * slot_depth, HD)
        returned = lax.all_to_all(result_block, "seq", split_axis=1, concat_axis=1, tiled=True)
        returned = returned.reshape(part_heads, CLUSTERS, n_head, slot_depth, HD)
        gathered = jnp.einsum(
            "hltcr,hclrd->lthd",
            home_table[half * part_heads:(half + 1) * part_heads],
            returned,
            preferred_element_type=jnp.float32,
        ).astype(jnp.bfloat16)
        gathered = gathered.reshape(tok_dev, part_heads * HD)
        projected.append(jnp.dot(
            gathered,
            weight[half * part_heads * HD:(half + 1) * part_heads * HD],
            preferred_element_type=jnp.float32,
        ))
    partial_value = projected[0]
    for part in projected[1:]:
        partial_value = partial_value + part
    return lax.psum_scatter(
        partial_value.astype(jnp.bfloat16), "head", scatter_dimension=1, tiled=True
    )


def solution(mesh):
    in_specs = (
        P(("seq", "head"), None),
        P(("seq", "head"), None),
        P(("seq", "head"), None),
        P(None, "seq", None),
        P("head", "seq"),
    )
    out_specs = P("seq", "head")
    return jax.shard_map(body, mesh=mesh, in_specs=in_specs, out_specs=out_specs, check_vma=False)
```

```python
import jax
import jax.numpy as jnp
from jax import lax
from jax.sharding import PartitionSpec as P

HEADS = 32
HD = 128
CLUSTERS = 128


def slot_table(block_ids, slot_depth):
    sub_rows = block_ids.shape[-1]
    onehot = (block_ids[..., None] == jnp.arange(CLUSTERS, dtype=jnp.int32)).astype(jnp.float32)
    lower = (jnp.arange(sub_rows)[:, None] >= jnp.arange(sub_rows)[None, :]).astype(jnp.float32)
    running = jnp.einsum("ts,abse->abte", lower, onehot)
    ranking = (jnp.sum(running * onehot, axis=-1) - 1.0).astype(jnp.int32)
    depth_hit = (ranking[..., None] == jnp.arange(slot_depth, dtype=jnp.int32)).astype(jnp.bfloat16)
    return onehot.astype(jnp.bfloat16)[..., :, None] * depth_hit[..., None, :]


def attend_blocks(query, key, value, validity):
    scores = jnp.einsum(
        "cqd,ckd->cqk", query, key, preferred_element_type=jnp.float32
    ) * HD ** (-0.5)
    scores = jnp.where(validity[:, None, :] > 0, scores, -1e30)
    row_max = jnp.max(scores, axis=-1, keepdims=True)
    raised = jnp.exp(scores - row_max)
    weights = (raised / jnp.sum(raised, axis=-1, keepdims=True)).astype(jnp.bfloat16)
    return jnp.einsum(
        "cqk,ckd->cqd", weights, value, preferred_element_type=jnp.float32
    ).astype(jnp.bfloat16)


def body(queries, keys, values, cluster_ids, out_weight):
    n_seq = lax.axis_size("seq")
    n_head = lax.axis_size("head")
    head_group = lax.axis_index("head")
    tok_dev = cluster_ids.shape[1]
    sub_rows = tok_dev // n_head
    group_heads = HEADS // n_head
    slot_depth = max(2, 2 * tok_dev // (n_head * CLUSTERS))
    per_owner = group_heads * CLUSTERS // n_seq
    n_src = n_seq * n_head
    all_ids = cluster_ids[:, :, 0]

    own_ids = lax.dynamic_slice_in_dim(all_ids, head_group * sub_rows, sub_rows, 1)
    own_table = slot_table(own_ids[:, None, :], slot_depth)[:, 0]
    stacked = jnp.stack([t.reshape(sub_rows, HEADS, HD) for t in (queries, keys, values)])
    packed = jnp.einsum(
        "htcr,xthd->xhcrd", own_table, stacked, preferred_element_type=jnp.float32
    ).astype(jnp.bfloat16)
    packed = packed.reshape(3, n_head, per_owner, n_seq, slot_depth, HD)
    packed = packed.transpose(0, 3, 1, 2, 4, 5).reshape(3, n_src, per_owner, slot_depth, HD)
    markers = jnp.sum(own_table.astype(jnp.float32), axis=1).astype(jnp.bfloat16)
    markers = markers.reshape(n_head, per_owner, n_seq, slot_depth)
    markers = markers.transpose(2, 0, 1, 3).reshape(n_src, per_owner, slot_depth)

    arrived = lax.all_to_all(packed, ("seq", "head"), split_axis=1, concat_axis=1, tiled=True)
    valid = lax.all_to_all(markers, ("seq", "head"), split_axis=0, concat_axis=0, tiled=True)
    arrived = arrived.transpose(0, 2, 1, 3, 4).reshape(3, per_owner, n_src * slot_depth, HD)
    valid = valid.transpose(1, 0, 2).reshape(per_owner, n_src * slot_depth)
    group_ids = lax.dynamic_slice_in_dim(all_ids, head_group * group_heads, group_heads, 0)
    group_ids = group_ids.reshape(group_heads, n_head, sub_rows)
    home_table = slot_table(group_ids, slot_depth)
    weight = lax.all_gather(out_weight, "seq", axis=1, tiled=True)

    halves = 2
    part_blocks = n_head // halves
    by_block = arrived.reshape(3, per_owner, n_seq, n_head, slot_depth, HD)
    outputs = []
    for half in range(halves):
        blocks = slice(half * part_blocks, (half + 1) * part_blocks)
        query = by_block[0, :, :, blocks].reshape(per_owner, -1, HD)
        result_block = attend_blocks(query, arrived[1], arrived[2], valid)
        result_block = result_block.reshape(per_owner, n_seq, part_blocks * slot_depth, HD)
        returned = lax.all_to_all(result_block, "seq", split_axis=1, concat_axis=1, tiled=True)
        returned = returned.reshape(group_heads, CLUSTERS, part_blocks, slot_depth, HD)
        gathered = jnp.einsum(
            "hltcr,hclrd->lthd", home_table[:, blocks], returned, preferred_element_type=jnp.float32
        ).astype(jnp.bfloat16)
        gathered = gathered.reshape(part_blocks * sub_rows, group_heads * HD)
        partial_value = jnp.dot(gathered, weight, preferred_element_type=jnp.float32)
        outputs.append(lax.psum_scatter(
            partial_value.astype(jnp.bfloat16), "head", scatter_dimension=1, tiled=True
        ))
    return jnp.concatenate(outputs, axis=0)


def solution(mesh):
    in_specs = (
        P(("seq", "head"), None),
        P(("seq", "head"), None),
        P(("seq", "head"), None),
        P(None, "seq", None),
        P("head", "seq"),
    )
    out_specs = P("seq", "head")
    return jax.shard_map(body, mesh=mesh, in_specs=in_specs, out_specs=out_specs, check_vma=False)
```

```python
import jax
import jax.numpy as jnp
from jax import lax
from jax.sharding import PartitionSpec as P

HEADS = 32
HD = 128
CLUSTERS = 128


def slot_table(block_ids, slot_depth):
    sub_rows = block_ids.shape[-1]
    onehot = (block_ids[..., None] == jnp.arange(CLUSTERS, dtype=jnp.int32)).astype(jnp.float32)
    lower = (jnp.arange(sub_rows)[:, None] >= jnp.arange(sub_rows)[None, :]).astype(jnp.float32)
    running = jnp.einsum("ts,abse->abte", lower, onehot)
    ranking = (jnp.sum(running * onehot, axis=-1) - 1.0).astype(jnp.int32)
    depth_hit = (ranking[..., None] == jnp.arange(slot_depth, dtype=jnp.int32)).astype(jnp.bfloat16)
    return onehot.astype(jnp.bfloat16)[..., :, None] * depth_hit[..., None, :]


def attend_blocks(packed, validity):
    scores = jnp.einsum(
        "cqd,ckd->cqk", packed[0], packed[1], preferred_element_type=jnp.float32
    ) * HD ** (-0.5)
    scores = jnp.where(validity[:, None, :], scores, -1e30)
    row_max = jnp.max(scores, axis=-1, keepdims=True)
    raised = jnp.exp(scores - row_max)
    weights = (raised / jnp.sum(raised, axis=-1, keepdims=True)).astype(jnp.bfloat16)
    return jnp.einsum(
        "cqk,ckd->cqd", weights, packed[2], preferred_element_type=jnp.float32
    ).astype(jnp.bfloat16)


def body(queries, keys, values, cluster_ids, out_weight):
    n_seq = lax.axis_size("seq")
    n_head = lax.axis_size("head")
    head_group = lax.axis_index("head")
    tok_dev = cluster_ids.shape[1]
    sub_rows = tok_dev // n_head
    group_heads = HEADS // n_head
    slot_depth = max(2, 2 * tok_dev // (n_head * CLUSTERS))
    per_owner = group_heads * CLUSTERS // n_seq
    n_src = n_seq * n_head
    all_ids = cluster_ids[:, :, 0]

    own_ids = lax.dynamic_slice_in_dim(all_ids, head_group * sub_rows, sub_rows, 1)
    own_table = slot_table(own_ids[:, None, :], slot_depth)[:, 0]
    stacked = jnp.stack([t.reshape(sub_rows, HEADS, HD) for t in (queries, keys, values)])
    packed = jnp.einsum(
        "htcr,xthd->xhcrd", own_table, stacked, preferred_element_type=jnp.float32
    ).astype(jnp.bfloat16)
    packed = packed.reshape(3, n_head, per_owner, n_seq, slot_depth, HD)
    packed = packed.transpose(0, 3, 1, 2, 4, 5).reshape(3, n_src, per_owner, slot_depth, HD)

    arrived = lax.all_to_all(packed, ("seq", "head"), split_axis=1, concat_axis=1, tiled=True)
    arrived = arrived.transpose(0, 2, 1, 3, 4).reshape(3, per_owner, n_src * slot_depth, HD)

    group_ids = lax.dynamic_slice_in_dim(all_ids, head_group * group_heads, group_heads, 0)
    seen_ids = lax.all_gather(group_ids, "seq", axis=1, tiled=True)
    seen_ids = seen_ids.reshape(group_heads, n_src, sub_rows)
    owned = jnp.arange(CLUSTERS // n_seq, dtype=jnp.int32) * n_seq + lax.axis_index("seq")
    counts = jnp.sum(
        (seen_ids[:, None, :, :] == owned[None, :, None, None]).astype(jnp.int32), axis=-1
    )
    counts = counts.reshape(per_owner, n_src)
    valid = counts[:, :, None] > jnp.arange(slot_depth, dtype=jnp.int32)
    valid = valid.reshape(per_owner, n_src * slot_depth)
    result_block = attend_blocks(arrived, valid)
    result_block = result_block.reshape(per_owner, n_seq, n_head * slot_depth, HD)
    returned = lax.all_to_all(result_block, "seq", split_axis=1, concat_axis=1, tiled=True)
    returned = returned.reshape(group_heads, CLUSTERS, n_head, slot_depth, HD)

    group_ids = group_ids.reshape(group_heads, n_head, sub_rows)
    home_table = slot_table(group_ids, slot_depth)
    gathered = jnp.einsum(
        "hltcr,hclrd->lthd", home_table, returned, preferred_element_type=jnp.float32
    ).astype(jnp.bfloat16)
    gathered = gathered.reshape(tok_dev, group_heads * HD)
    partial_value = jnp.dot(
        gathered,
        lax.all_gather(out_weight, "seq", axis=1, tiled=True),
        preferred_element_type=jnp.float32,
    )
    return lax.psum_scatter(
        partial_value.astype(jnp.bfloat16), "head", scatter_dimension=1, tiled=True
    )


def solution(mesh):
    in_specs = (
        P(("seq", "head"), None),
        P(("seq", "head"), None),
        P(("seq", "head"), None),
        P(None, "seq", None),
        P("head", "seq"),
    )
    out_specs = P("seq", "head")
    return jax.shard_map(body, mesh=mesh, in_specs=in_specs, out_specs=out_specs, check_vma=False)
```

```python
import jax
import jax.numpy as jnp
from jax import lax
from jax.sharding import PartitionSpec as P

HEADS = 32
HD = 128
CLUSTERS = 128


def slot_table(block_ids, slot_depth):
    sub_rows = block_ids.shape[-1]
    onehot = (block_ids[..., None] == jnp.arange(CLUSTERS, dtype=jnp.int32)).astype(jnp.float32)
    lower = (jnp.arange(sub_rows)[:, None] >= jnp.arange(sub_rows)[None, :]).astype(jnp.float32)
    running = jnp.einsum("ts,abse->abte", lower, onehot)
    ranking = (jnp.sum(running * onehot, axis=-1) - 1.0).astype(jnp.int32)
    depth_hit = (ranking[..., None] == jnp.arange(slot_depth, dtype=jnp.int32)).astype(jnp.bfloat16)
    return onehot.astype(jnp.bfloat16)[..., :, None] * depth_hit[..., None, :]


def attend_blocks(packed, validity):
    scores = jnp.einsum(
        "cqd,ckd->cqk", packed[0], packed[1], preferred_element_type=jnp.float32
    ) * HD ** (-0.5)
    scores = jnp.where(validity[:, None, :], scores, -1e30)
    row_max = jnp.max(scores, axis=-1, keepdims=True)
    raised = jnp.exp(scores - row_max)
    weights = (raised / jnp.sum(raised, axis=-1, keepdims=True)).astype(jnp.bfloat16)
    return jnp.einsum(
        "cqk,ckd->cqd", weights, packed[2], preferred_element_type=jnp.float32
    ).astype(jnp.bfloat16)


def body(queries, keys, values, cluster_ids, out_weight):
    n_seq = lax.axis_size("seq")
    n_head = lax.axis_size("head")
    head_group = lax.axis_index("head")
    tok_dev = cluster_ids.shape[1]
    sub_rows = tok_dev // n_head
    group_heads = HEADS // n_head
    slot_depth = max(2, 2 * tok_dev // (n_head * CLUSTERS))
    per_owner = group_heads * CLUSTERS // n_seq
    n_src = n_seq * n_head
    all_ids = cluster_ids[:, :, 0]

    own_ids = lax.dynamic_slice_in_dim(all_ids, head_group * sub_rows, sub_rows, 1)
    own_table = slot_table(own_ids[:, None, :], slot_depth)[:, 0]
    stacked = jnp.stack([t.reshape(sub_rows, n_head, group_heads, HD) for t in (queries, keys, values)])
    own_table = own_table.reshape(
        n_head, group_heads, sub_rows, CLUSTERS // n_seq, n_seq, slot_depth
    )
    packed = jnp.einsum(
        "gjtacr,xtgjd->cgxjard", own_table, stacked, preferred_element_type=jnp.float32
    ).astype(jnp.bfloat16)
    packed = packed.reshape(n_src, 3, per_owner, slot_depth, HD)

    arrived = lax.all_to_all(packed, ("seq", "head"), split_axis=0, concat_axis=0, tiled=True)
    arrived = arrived.transpose(1, 2, 0, 3, 4).reshape(3, per_owner, n_src * slot_depth, HD)

    group_ids = lax.dynamic_slice_in_dim(all_ids, head_group * group_heads, group_heads, 0)
    seen_ids = lax.all_gather(group_ids, "seq", axis=1, tiled=True)
    seen_ids = seen_ids.reshape(group_heads, n_src, sub_rows)
    owned = jnp.arange(CLUSTERS // n_seq, dtype=jnp.int32) * n_seq + lax.axis_index("seq")
    counts = jnp.sum(
        (seen_ids[:, None, :, :] == owned[None, :, None, None]).astype(jnp.int32), axis=-1
    )
    counts = counts.reshape(per_owner, n_src)
    valid = counts[:, :, None] > jnp.arange(slot_depth, dtype=jnp.int32)
    valid = valid.reshape(per_owner, n_src * slot_depth)
    result_block = attend_blocks(arrived, valid)
    result_block = result_block.reshape(per_owner, n_seq, n_head * slot_depth, HD)
    returned = lax.all_to_all(result_block, "seq", split_axis=1, concat_axis=1, tiled=True)
    returned = returned.reshape(group_heads, CLUSTERS, n_head, slot_depth, HD)

    group_ids = group_ids.reshape(group_heads, n_head, sub_rows)
    home_table = slot_table(group_ids, slot_depth)
    gathered = jnp.einsum(
        "hltcr,hclrd->lthd", home_table, returned, preferred_element_type=jnp.float32
    ).astype(jnp.bfloat16)
    gathered = gathered.reshape(tok_dev, group_heads * HD)
    partial_value = jnp.dot(
        gathered,
        lax.all_gather(out_weight, "seq", axis=1, tiled=True),
        preferred_element_type=jnp.float32,
    )
    return lax.psum_scatter(
        partial_value.astype(jnp.bfloat16), "head", scatter_dimension=1, tiled=True
    )


def solution(mesh):
    in_specs = (
        P(("seq", "head"), None),
        P(("seq", "head"), None),
        P(("seq", "head"), None),
        P(None, "seq", None),
        P("head", "seq"),
    )
    out_specs = P("seq", "head")
    return jax.shard_map(body, mesh=mesh, in_specs=in_specs, out_specs=out_specs, check_vma=False)
```

```python
import jax
import jax.numpy as jnp
from jax import lax
from jax.experimental import pallas as pl
from jax.sharding import PartitionSpec as P

HEADS = 32
HD = 128
CLUSTERS = 128


def slot_table(block_ids, slot_depth):
    sub_rows = block_ids.shape[-1]
    onehot = (block_ids[..., None] == jnp.arange(CLUSTERS, dtype=jnp.int32)).astype(jnp.float32)
    lower = (jnp.arange(sub_rows)[:, None] >= jnp.arange(sub_rows)[None, :]).astype(jnp.float32)
    running = jnp.einsum("ts,abse->abte", lower, onehot)
    ranking = (jnp.sum(running * onehot, axis=-1) - 1.0).astype(jnp.int32)
    depth_hit = (ranking[..., None] == jnp.arange(slot_depth, dtype=jnp.int32)).astype(jnp.bfloat16)
    return onehot.astype(jnp.bfloat16)[..., :, None] * depth_hit[..., None, :]


def attend_kernel(q_ref, k_ref, v_ref, mask_ref, out_ref):
    scores = lax.dot_general(
        q_ref[0], k_ref[0], (((1,), (1,)), ((), ())), preferred_element_type=jnp.float32
    ) * HD ** (-0.5)
    scores = jnp.where(mask_ref[0] > 0, scores, -1e30)
    row_max = jnp.max(scores, axis=-1, keepdims=True)
    raised = jnp.exp(scores - row_max)
    weights = (raised / jnp.sum(raised, axis=-1, keepdims=True)).astype(jnp.bfloat16)
    out_ref[0] = jnp.dot(weights, v_ref[0], preferred_element_type=jnp.float32).astype(out_ref.dtype)


def attend_blocks(packed, validity):
    items, slots, _ = packed.shape[1:]
    mask = validity.astype(jnp.float32).reshape(items, 1, slots)
    row_spec = pl.BlockSpec((1, slots, HD), lambda i: (i, 0, 0))
    return pl.pallas_call(
        attend_kernel,
        grid=(items,),
        in_specs=[row_spec, row_spec, row_spec, pl.BlockSpec((1, 1, slots), lambda i: (i, 0, 0))],
        out_specs=row_spec,
        out_shape=jax.ShapeDtypeStruct((items, slots, HD), jnp.bfloat16),
        cost_estimate=pl.CostEstimate(
            flops=4 * items * slots * slots * HD,
            transcendentals=items * slots * slots,
            bytes_accessed=4 * items * slots * HD * 2,
        ),
    )(packed[0], packed[1], packed[2], mask)


def body(queries, keys, values, cluster_ids, out_weight):
    n_seq = lax.axis_size("seq")
    n_head = lax.axis_size("head")
    head_group = lax.axis_index("head")
    tok_dev = cluster_ids.shape[1]
    sub_rows = tok_dev // n_head
    group_heads = HEADS // n_head
    slot_depth = max(2, 2 * tok_dev // (n_head * CLUSTERS))
    per_owner = group_heads * CLUSTERS // n_seq
    n_src = n_seq * n_head
    all_ids = cluster_ids[:, :, 0]

    own_ids = lax.dynamic_slice_in_dim(all_ids, head_group * sub_rows, sub_rows, 1)
    own_table = slot_table(own_ids[:, None, :], slot_depth)[:, 0]
    stacked = jnp.stack([t.reshape(sub_rows, HEADS, HD) for t in (queries, keys, values)])
    packed = jnp.einsum(
        "htcr,xthd->xhcrd", own_table, stacked, preferred_element_type=jnp.float32
    ).astype(jnp.bfloat16)
    packed = packed.reshape(3, n_head, per_owner, n_seq, slot_depth, HD)
    packed = packed.transpose(0, 3, 1, 2, 4, 5).reshape(3, n_src, per_owner, slot_depth, HD)

    arrived = lax.all_to_all(packed, ("seq", "head"), split_axis=1, concat_axis=1, tiled=True)
    arrived = arrived.transpose(0, 2, 1, 3, 4).reshape(3, per_owner, n_src * slot_depth, HD)

    group_ids = lax.dynamic_slice_in_dim(all_ids, head_group * group_heads, group_heads, 0)
    seen_ids = lax.all_gather(group_ids, "seq", axis=1, tiled=True)
    seen_ids = seen_ids.reshape(group_heads, n_src, sub_rows)
    owned = jnp.arange(CLUSTERS // n_seq, dtype=jnp.int32) * n_seq + lax.axis_index("seq")
    counts = jnp.sum(
        (seen_ids[:, None, :, :] == owned[None, :, None, None]).astype(jnp.int32), axis=-1
    )
    counts = counts.reshape(per_owner, n_src)
    valid = counts[:, :, None] > jnp.arange(slot_depth, dtype=jnp.int32)
    valid = valid.reshape(per_owner, n_src * slot_depth)
    result_block = attend_blocks(arrived, valid)
    result_block = result_block.reshape(per_owner, n_seq, n_head * slot_depth, HD)
    returned = lax.all_to_all(result_block, "seq", split_axis=1, concat_axis=1, tiled=True)
    returned = returned.reshape(group_heads, CLUSTERS, n_head, slot_depth, HD)

    group_ids = group_ids.reshape(group_heads, n_head, sub_rows)
    home_table = slot_table(group_ids, slot_depth)
    gathered = jnp.einsum(
        "hltcr,hclrd->lthd", home_table, returned, preferred_element_type=jnp.float32
    ).astype(jnp.bfloat16)
    gathered = gathered.reshape(tok_dev, group_heads * HD)
    partial_value = jnp.dot(
        gathered,
        lax.all_gather(out_weight, "seq", axis=1, tiled=True),
        preferred_element_type=jnp.float32,
    )
    return lax.psum_scatter(
        partial_value.astype(jnp.bfloat16), "head", scatter_dimension=1, tiled=True
    )


def solution(mesh):
    in_specs = (
        P(("seq", "head"), None),
        P(("seq", "head"), None),
        P(("seq", "head"), None),
        P(None, "seq", None),
        P("head", "seq"),
    )
    out_specs = P("seq", "head")
    return jax.shard_map(body, mesh=mesh, in_specs=in_specs, out_specs=out_specs, check_vma=False)
```

```python
import jax
import jax.numpy as jnp
from jax import lax
from jax.experimental import pallas as pl
from jax.sharding import PartitionSpec as P

HEADS = 32
HD = 128
CLUSTERS = 128


def slot_table(block_ids, slot_depth):
    sub_rows = block_ids.shape[-1]
    onehot = (block_ids[..., None] == jnp.arange(CLUSTERS, dtype=jnp.int32)).astype(jnp.float32)
    lower = (jnp.arange(sub_rows)[:, None] >= jnp.arange(sub_rows)[None, :]).astype(jnp.float32)
    running = jnp.einsum("ts,abse->abte", lower, onehot)
    ranking = (jnp.sum(running * onehot, axis=-1) - 1.0).astype(jnp.int32)
    depth_hit = (ranking[..., None] == jnp.arange(slot_depth, dtype=jnp.int32)).astype(jnp.bfloat16)
    return onehot.astype(jnp.bfloat16)[..., :, None] * depth_hit[..., None, :]


def attend_kernel(q_ref, k_ref, v_ref, mask_ref, out_ref):
    scores = lax.dot_general(
        q_ref[0], k_ref[0], (((1,), (1,)), ((), ())), preferred_element_type=jnp.float32
    ) * HD ** (-0.5)
    scores = jnp.where(mask_ref[0] > 0, scores, -1e30)
    row_max = jnp.max(scores, axis=-1, keepdims=True)
    raised = jnp.exp(scores - row_max)
    weights = (raised / jnp.sum(raised, axis=-1, keepdims=True)).astype(jnp.bfloat16)
    result = jnp.dot(weights, v_ref[0], preferred_element_type=jnp.float32)
    out_ref[:, 0] = result.reshape(out_ref.shape[0], out_ref.shape[2], HD).astype(out_ref.dtype)


def attend_blocks(packed, validity, n_dest):
    items, slots, _ = packed.shape[1:]
    lanes = slots // n_dest
    mask = validity.astype(jnp.float32).reshape(items, 1, slots)
    row_spec = pl.BlockSpec((1, slots, HD), lambda i: (i, 0, 0))
    return pl.pallas_call(
        attend_kernel,
        grid=(items,),
        in_specs=[row_spec, row_spec, row_spec, pl.BlockSpec((1, 1, slots), lambda i: (i, 0, 0))],
        out_specs=pl.BlockSpec((n_dest, 1, lanes, HD), lambda i: (0, i, 0, 0)),
        out_shape=jax.ShapeDtypeStruct((n_dest, items, lanes, HD), jnp.bfloat16),
        cost_estimate=pl.CostEstimate(
            flops=4 * items * slots * slots * HD,
            transcendentals=items * slots * slots,
            bytes_accessed=4 * items * slots * HD * 2,
        ),
    )(packed[0], packed[1], packed[2], mask)


def body(queries, keys, values, cluster_ids, out_weight):
    n_seq = lax.axis_size("seq")
    n_head = lax.axis_size("head")
    head_group = lax.axis_index("head")
    tok_dev = cluster_ids.shape[1]
    sub_rows = tok_dev // n_head
    group_heads = HEADS // n_head
    slot_depth = max(2, 2 * tok_dev // (n_head * CLUSTERS))
    per_owner = group_heads * CLUSTERS // n_seq
    n_src = n_seq * n_head
    all_ids = cluster_ids[:, :, 0]

    own_ids = lax.dynamic_slice_in_dim(all_ids, head_group * sub_rows, sub_rows, 1)
    own_table = slot_table(own_ids[:, None, :], slot_depth)[:, 0]
    stacked = jnp.stack([t.reshape(sub_rows, HEADS, HD) for t in (queries, keys, values)])
    packed = jnp.einsum(
        "htcr,xthd->xhcrd", own_table, stacked, preferred_element_type=jnp.float32
    ).astype(jnp.bfloat16)
    packed = packed.reshape(3, n_head, per_owner, n_seq, slot_depth, HD)
    packed = packed.transpose(0, 3, 1, 2, 4, 5).reshape(3, n_src, per_owner, slot_depth, HD)

    group_ids = lax.dynamic_slice_in_dim(cluster_ids, head_group * group_heads, group_heads, 0)
    group_ids, packed = lax.optimization_barrier((group_ids, packed))
    arrived = lax.all_to_all(packed, ("seq", "head"), split_axis=1, concat_axis=1, tiled=True)
    arrived = arrived.transpose(0, 2, 1, 3, 4).reshape(3, per_owner, n_src * slot_depth, HD)

    seen_ids = lax.all_gather(group_ids, "seq", axis=1, tiled=True)
    seen_ids = seen_ids.reshape(group_heads, n_src, sub_rows)
    group_ids = group_ids[:, :, 0]
    owned = jnp.arange(CLUSTERS // n_seq, dtype=jnp.int32) * n_seq + lax.axis_index("seq")
    counts = jnp.sum(
        (seen_ids[:, None, :, :] == owned[None, :, None, None]).astype(jnp.int32), axis=-1
    )
    counts = counts.reshape(per_owner, n_src)
    valid = counts[:, :, None] > jnp.arange(slot_depth, dtype=jnp.int32)
    valid = valid.reshape(per_owner, n_src * slot_depth)
    result_block = attend_blocks(arrived, valid, n_seq)
    returned = lax.all_to_all(result_block, "seq", split_axis=0, concat_axis=0, tiled=True)
    returned = returned.transpose(1, 0, 2, 3).reshape(group_heads, CLUSTERS, n_head, slot_depth, HD)

    group_ids = group_ids.reshape(group_heads, n_head, sub_rows)
    home_table = slot_table(group_ids, slot_depth)
    gathered = jnp.einsum(
        "hltcr,hclrd->lthd", home_table, returned, preferred_element_type=jnp.float32
    ).astype(jnp.bfloat16)
    gathered = gathered.reshape(tok_dev, group_heads * HD)
    partial_value = jnp.dot(
        gathered,
        lax.all_gather(out_weight, "seq", axis=1, tiled=True),
        preferred_element_type=jnp.float32,
    )
    return lax.psum_scatter(
        partial_value.astype(jnp.bfloat16), "head", scatter_dimension=1, tiled=True
    )


def solution(mesh):
    in_specs = (
        P(("seq", "head"), None),
        P(("seq", "head"), None),
        P(("seq", "head"), None),
        P(None, "seq", None),
        P("head", "seq"),
    )
    out_specs = P("seq", "head")
    return jax.shard_map(body, mesh=mesh, in_specs=in_specs, out_specs=out_specs, check_vma=False)
```

```python
import jax
import jax.numpy as jnp
from jax import lax
from jax.experimental import pallas as pl
from jax.sharding import PartitionSpec as P

HEADS = 32
HD = 128
CLUSTERS = 128


def slot_table(block_ids, slot_depth):
    sub_rows = block_ids.shape[-1]
    onehot = (block_ids[..., None] == jnp.arange(CLUSTERS, dtype=jnp.int32)).astype(jnp.float32)
    lower = (jnp.arange(sub_rows)[:, None] >= jnp.arange(sub_rows)[None, :]).astype(jnp.float32)
    running = jnp.einsum("ts,abse->abte", lower, onehot)
    ranking = (jnp.sum(running * onehot, axis=-1) - 1.0).astype(jnp.int32)
    depth_hit = (ranking[..., None] == jnp.arange(slot_depth, dtype=jnp.int32)).astype(jnp.bfloat16)
    return onehot.astype(jnp.bfloat16)[..., :, None] * depth_hit[..., None, :]


def attend_kernel(q_ref, k_ref, v_ref, mask_ref, out_ref):
    scores = lax.dot_general(
        q_ref[0], k_ref[0], (((1,), (1,)), ((), ())), preferred_element_type=jnp.float32
    ) * HD ** (-0.5)
    scores = jnp.where(mask_ref[0] > 0, scores, -1e30)
    row_max = jnp.max(scores, axis=-1, keepdims=True)
    raised = jnp.exp(scores - row_max)
    weights = (raised / jnp.sum(raised, axis=-1, keepdims=True)).astype(jnp.bfloat16)
    result = jnp.dot(weights, v_ref[0], preferred_element_type=jnp.float32)
    out_ref[:, 0] = result.reshape(out_ref.shape[0], out_ref.shape[2], HD).astype(out_ref.dtype)


def attend_blocks(packed, validity, n_dest):
    items, slots, _ = packed.shape[1:]
    lanes = slots // n_dest
    mask = validity.astype(jnp.float32).reshape(items, 1, slots)
    row_spec = pl.BlockSpec((1, slots, HD), lambda i: (i, 0, 0))
    return pl.pallas_call(
        attend_kernel,
        grid=(items,),
        in_specs=[row_spec, row_spec, row_spec, pl.BlockSpec((1, 1, slots), lambda i: (i, 0, 0))],
        out_specs=pl.BlockSpec((n_dest, 1, lanes, HD), lambda i: (0, i, 0, 0)),
        out_shape=jax.ShapeDtypeStruct((n_dest, items, lanes, HD), jnp.bfloat16),
        cost_estimate=pl.CostEstimate(
            flops=40 * items * slots * slots * HD,
            transcendentals=10 * items * slots * slots,
            bytes_accessed=4 * items * slots * HD * 2,
        ),
    )(packed[0], packed[1], packed[2], mask)


def body(queries, keys, values, cluster_ids, out_weight):
    n_seq = lax.axis_size("seq")
    n_head = lax.axis_size("head")
    head_group = lax.axis_index("head")
    tok_dev = cluster_ids.shape[1]
    sub_rows = tok_dev // n_head
    group_heads = HEADS // n_head
    slot_depth = max(2, 2 * tok_dev // (n_head * CLUSTERS))
    per_owner = group_heads * CLUSTERS // n_seq
    n_src = n_seq * n_head
    all_ids = cluster_ids[:, :, 0]

    own_ids = lax.dynamic_slice_in_dim(all_ids, head_group * sub_rows, sub_rows, 1)
    own_table = slot_table(own_ids[:, None, :], slot_depth)[:, 0]
    stacked = jnp.stack([t.reshape(sub_rows, HEADS, HD) for t in (queries, keys, values)])
    packed = jnp.einsum(
        "htcr,xthd->xhcrd", own_table, stacked, preferred_element_type=jnp.float32
    ).astype(jnp.bfloat16)
    packed = packed.reshape(3, n_head, per_owner, n_seq, slot_depth, HD)
    packed = packed.transpose(0, 3, 1, 2, 4, 5).reshape(3, n_src, per_owner, slot_depth, HD)

    group_ids = lax.dynamic_slice_in_dim(cluster_ids, head_group * group_heads, group_heads, 0)
    arrived = lax.all_to_all(packed, ("seq", "head"), split_axis=1, concat_axis=1, tiled=True)
    arrived = arrived.transpose(0, 2, 1, 3, 4).reshape(3, per_owner, n_src * slot_depth, HD)

    seen_ids = lax.all_gather(group_ids, "seq", axis=1, tiled=True)
    seen_ids = seen_ids.reshape(group_heads, n_src, sub_rows)
    group_ids = group_ids[:, :, 0]
    owned = jnp.arange(CLUSTERS // n_seq, dtype=jnp.int32) * n_seq + lax.axis_index("seq")
    counts = jnp.sum(
        (seen_ids[:, None, :, :] == owned[None, :, None, None]).astype(jnp.int32), axis=-1
    )
    counts = counts.reshape(per_owner, n_src)
    valid = counts[:, :, None] > jnp.arange(slot_depth, dtype=jnp.int32)
    valid = valid.reshape(per_owner, n_src * slot_depth)
    result_block = attend_blocks(arrived, valid, n_seq)
    returned = lax.all_to_all(result_block, "seq", split_axis=0, concat_axis=0, tiled=True)
    returned = returned.transpose(1, 0, 2, 3).reshape(group_heads, CLUSTERS, n_head, slot_depth, HD)

    group_ids = group_ids.reshape(group_heads, n_head, sub_rows)
    home_table = slot_table(group_ids, slot_depth)
    gathered = jnp.einsum(
        "hltcr,hclrd->lthd", home_table, returned, preferred_element_type=jnp.float32
    ).astype(jnp.bfloat16)
    gathered = gathered.reshape(tok_dev, group_heads * HD)
    partial_value = jnp.dot(
        gathered,
        lax.all_gather(out_weight, "seq", axis=1, tiled=True),
        preferred_element_type=jnp.float32,
    )
    return lax.psum_scatter(
        partial_value.astype(jnp.bfloat16), "head", scatter_dimension=1, tiled=True
    )


def solution(mesh):
    in_specs = (
        P(("seq", "head"), None),
        P(("seq", "head"), None),
        P(("seq", "head"), None),
        P(None, "seq", None),
        P("head", "seq"),
    )
    out_specs = P("seq", "head")
    return jax.shard_map(body, mesh=mesh, in_specs=in_specs, out_specs=out_specs, check_vma=False)
```

```python
import jax
import jax.numpy as jnp
from jax import lax
from jax.experimental import pallas as pl
from jax.sharding import PartitionSpec as P

HEADS = 32
HD = 128
CLUSTERS = 128


def slot_table(block_ids, slot_depth):
    sub_rows = block_ids.shape[-1]
    onehot = (block_ids[..., None] == jnp.arange(CLUSTERS, dtype=jnp.int32)).astype(jnp.float32)
    lower = (jnp.arange(sub_rows)[:, None] >= jnp.arange(sub_rows)[None, :]).astype(jnp.float32)
    running = jnp.einsum("ts,abse->abte", lower, onehot)
    ranking = (jnp.sum(running * onehot, axis=-1) - 1.0).astype(jnp.int32)
    depth_hit = (ranking[..., None] == jnp.arange(slot_depth, dtype=jnp.int32)).astype(jnp.bfloat16)
    return onehot.astype(jnp.bfloat16)[..., :, None] * depth_hit[..., None, :]


def attend_kernel(q_ref, k_ref, v_ref, mask_ref, out_ref):
    scores = lax.dot_general(
        q_ref[0, 0], k_ref[0, 0], (((1,), (1,)), ((), ())), preferred_element_type=jnp.float32
    ) * HD ** (-0.5)
    scores = jnp.where(mask_ref[0] > 0, scores, -1e30)
    row_max = jnp.max(scores, axis=-1, keepdims=True)
    raised = jnp.exp(scores - row_max)
    weights = (raised / jnp.sum(raised, axis=-1, keepdims=True)).astype(jnp.bfloat16)
    result = jnp.dot(weights, v_ref[0, 0], preferred_element_type=jnp.float32)
    out_ref[:, 0] = result.reshape(out_ref.shape[0], out_ref.shape[2], HD).astype(out_ref.dtype)


def attend_blocks(packed, validity, n_dest):
    items, slots, _ = packed.shape[1:]
    lanes = slots // n_dest
    mask = validity.astype(jnp.float32).reshape(items, 1, slots)
    specs = [pl.BlockSpec((1, 1, slots, HD), lambda i, x=x: (x, i, 0, 0)) for x in range(3)]
    return pl.pallas_call(
        attend_kernel,
        grid=(items,),
        in_specs=specs + [pl.BlockSpec((1, 1, slots), lambda i: (i, 0, 0))],
        out_specs=pl.BlockSpec((n_dest, 1, lanes, HD), lambda i: (0, i, 0, 0)),
        out_shape=jax.ShapeDtypeStruct((n_dest, items, lanes, HD), jnp.bfloat16),
        cost_estimate=pl.CostEstimate(
            flops=40 * items * slots * slots * HD,
            transcendentals=10 * items * slots * slots,
            bytes_accessed=4 * items * slots * HD * 2,
        ),
    )(packed, packed, packed, mask)


def body(queries, keys, values, cluster_ids, out_weight):
    n_seq = lax.axis_size("seq")
    n_head = lax.axis_size("head")
    head_group = lax.axis_index("head")
    tok_dev = cluster_ids.shape[1]
    sub_rows = tok_dev // n_head
    group_heads = HEADS // n_head
    slot_depth = max(2, 2 * tok_dev // (n_head * CLUSTERS))
    per_owner = group_heads * CLUSTERS // n_seq
    n_src = n_seq * n_head
    all_ids = cluster_ids[:, :, 0]

    own_ids = lax.dynamic_slice_in_dim(all_ids, head_group * sub_rows, sub_rows, 1)
    own_table = slot_table(own_ids[:, None, :], slot_depth)[:, 0]
    stacked = jnp.stack([t.reshape(sub_rows, HEADS, HD) for t in (queries, keys, values)])
    packed = jnp.einsum(
        "htcr,xthd->xhcrd", own_table, stacked, preferred_element_type=jnp.float32
    ).astype(jnp.bfloat16)
    packed = packed.reshape(3, n_head, per_owner, n_seq, slot_depth, HD)
    packed = packed.transpose(0, 3, 1, 2, 4, 5).reshape(3, n_src, per_owner, slot_depth, HD)

    group_ids = lax.dynamic_slice_in_dim(cluster_ids, head_group * group_heads, group_heads, 0)
    arrived = lax.all_to_all(packed, ("seq", "head"), split_axis=1, concat_axis=1, tiled=True)
    arrived = arrived.transpose(0, 2, 1, 3, 4).reshape(3, per_owner, n_src * slot_depth, HD)

    seen_ids = lax.all_gather(group_ids, "seq", axis=1, tiled=True)
    seen_ids = seen_ids.reshape(group_heads, n_src, sub_rows)
    group_ids = group_ids[:, :, 0]
    owned = jnp.arange(CLUSTERS // n_seq, dtype=jnp.int32) * n_seq + lax.axis_index("seq")
    counts = jnp.sum(
        (seen_ids[:, None, :, :] == owned[None, :, None, None]).astype(jnp.int32), axis=-1
    )
    counts = counts.reshape(per_owner, n_src)
    valid = counts[:, :, None] > jnp.arange(slot_depth, dtype=jnp.int32)
    valid = valid.reshape(per_owner, n_src * slot_depth)
    result_block = attend_blocks(arrived, valid, n_seq)
    returned = lax.all_to_all(result_block, "seq", split_axis=0, concat_axis=0, tiled=True)
    returned = returned.transpose(1, 0, 2, 3).reshape(group_heads, CLUSTERS, n_head, slot_depth, HD)

    group_ids = group_ids.reshape(group_heads, n_head, sub_rows)
    home_table = slot_table(group_ids, slot_depth)
    gathered = jnp.einsum(
        "hltcr,hclrd->lthd", home_table, returned, preferred_element_type=jnp.float32
    ).astype(jnp.bfloat16)
    gathered = gathered.reshape(tok_dev, group_heads * HD)
    partial_value = jnp.dot(
        gathered,
        lax.all_gather(out_weight, "seq", axis=1, tiled=True),
        preferred_element_type=jnp.float32,
    )
    return lax.psum_scatter(
        partial_value.astype(jnp.bfloat16), "head", scatter_dimension=1, tiled=True
    )


def solution(mesh):
    in_specs = (
        P(("seq", "head"), None),
        P(("seq", "head"), None),
        P(("seq", "head"), None),
        P(None, "seq", None),
        P("head", "seq"),
    )
    out_specs = P("seq", "head")
    return jax.shard_map(body, mesh=mesh, in_specs=in_specs, out_specs=out_specs, check_vma=False)
```

```python
import jax
import jax.numpy as jnp
from jax import lax
from jax.experimental import pallas as pl
from jax.sharding import PartitionSpec as P

HEADS = 32
HD = 128
CLUSTERS = 128


def slot_table(block_ids, slot_depth):
    sub_rows = block_ids.shape[-1]
    onehot = (block_ids[..., None] == jnp.arange(CLUSTERS, dtype=jnp.int32)).astype(jnp.float32)
    lower = (jnp.arange(sub_rows)[:, None] >= jnp.arange(sub_rows)[None, :]).astype(jnp.float32)
    running = jnp.einsum("ts,abse->abte", lower, onehot)
    ranking = (jnp.sum(running * onehot, axis=-1) - 1.0).astype(jnp.int32)
    depth_hit = (ranking[..., None] == jnp.arange(slot_depth, dtype=jnp.int32)).astype(jnp.bfloat16)
    return onehot.astype(jnp.bfloat16)[..., :, None] * depth_hit[..., None, :]


def attend_kernel(q_ref, k_ref, v_ref, mask_ref, out_ref):
    for item in range(q_ref.shape[1]):
        scores = lax.dot_general(
            q_ref[0, item], k_ref[0, item], (((1,), (1,)), ((), ())),
            preferred_element_type=jnp.float32,
        ) * HD ** (-0.5)
        scores = jnp.where(mask_ref[item] > 0, scores, -1e30)
        row_max = jnp.max(scores, axis=-1, keepdims=True)
        raised = jnp.exp(scores - row_max)
        weights = (raised / jnp.sum(raised, axis=-1, keepdims=True)).astype(jnp.bfloat16)
        result = jnp.dot(weights, v_ref[0, item], preferred_element_type=jnp.float32)
        out_ref[:, item] = result.reshape(out_ref.shape[0], out_ref.shape[2], HD).astype(out_ref.dtype)


def attend_blocks(packed, validity, n_dest):
    items, slots, _ = packed.shape[1:]
    lanes = slots // n_dest
    mask = validity.astype(jnp.float32).reshape(items, 1, slots)
    step = 2
    specs = [pl.BlockSpec((1, step, slots, HD), lambda i, x=x: (x, i, 0, 0)) for x in range(3)]
    return pl.pallas_call(
        attend_kernel,
        grid=(items // step,),
        in_specs=specs + [pl.BlockSpec((step, 1, slots), lambda i: (i, 0, 0))],
        out_specs=pl.BlockSpec((n_dest, step, lanes, HD), lambda i: (0, i, 0, 0)),
        out_shape=jax.ShapeDtypeStruct((n_dest, items, lanes, HD), jnp.bfloat16),
        cost_estimate=pl.CostEstimate(
            flops=40 * items * slots * slots * HD,
            transcendentals=10 * items * slots * slots,
            bytes_accessed=4 * items * slots * HD * 2,
        ),
    )(packed, packed, packed, mask)


def body(queries, keys, values, cluster_ids, out_weight):
    n_seq = lax.axis_size("seq")
    n_head = lax.axis_size("head")
    head_group = lax.axis_index("head")
    tok_dev = cluster_ids.shape[1]
    sub_rows = tok_dev // n_head
    group_heads = HEADS // n_head
    slot_depth = max(2, 2 * tok_dev // (n_head * CLUSTERS))
    per_owner = group_heads * CLUSTERS // n_seq
    n_src = n_seq * n_head
    all_ids = cluster_ids[:, :, 0]

    own_ids = lax.dynamic_slice_in_dim(all_ids, head_group * sub_rows, sub_rows, 1)
    own_table = slot_table(own_ids[:, None, :], slot_depth)[:, 0]
    stacked = jnp.stack([t.reshape(sub_rows, HEADS, HD) for t in (queries, keys, values)])
    packed = jnp.einsum(
        "htcr,xthd->xhcrd", own_table, stacked, preferred_element_type=jnp.float32
    ).astype(jnp.bfloat16)
    packed = packed.reshape(3, n_head, per_owner, n_seq, slot_depth, HD)
    packed = packed.transpose(0, 3, 1, 2, 4, 5).reshape(3, n_src, per_owner, slot_depth, HD)

    group_ids = lax.dynamic_slice_in_dim(cluster_ids, head_group * group_heads, group_heads, 0)
    arrived = lax.all_to_all(packed, ("seq", "head"), split_axis=1, concat_axis=1, tiled=True)
    arrived = arrived.transpose(0, 2, 1, 3, 4).reshape(3, per_owner, n_src * slot_depth, HD)

    seen_ids = lax.all_gather(group_ids, "seq", axis=1, tiled=True)
    seen_ids = seen_ids.reshape(group_heads, n_src, sub_rows)
    group_ids = group_ids[:, :, 0]
    owned = jnp.arange(CLUSTERS // n_seq, dtype=jnp.int32) * n_seq + lax.axis_index("seq")
    counts = jnp.sum(
        (seen_ids[:, None, :, :] == owned[None, :, None, None]).astype(jnp.int32), axis=-1
    )
    counts = counts.reshape(per_owner, n_src)
    valid = counts[:, :, None] > jnp.arange(slot_depth, dtype=jnp.int32)
    valid = valid.reshape(per_owner, n_src * slot_depth)
    result_block = attend_blocks(arrived, valid, n_seq)
    returned = lax.all_to_all(result_block, "seq", split_axis=0, concat_axis=0, tiled=True)
    returned = returned.transpose(1, 0, 2, 3).reshape(group_heads, CLUSTERS, n_head, slot_depth, HD)

    group_ids = group_ids.reshape(group_heads, n_head, sub_rows)
    home_table = slot_table(group_ids, slot_depth)
    gathered = jnp.einsum(
        "hltcr,hclrd->lthd", home_table, returned, preferred_element_type=jnp.float32
    ).astype(jnp.bfloat16)
    gathered = gathered.reshape(tok_dev, group_heads * HD)
    partial_value = jnp.dot(
        gathered,
        lax.all_gather(out_weight, "seq", axis=1, tiled=True),
        preferred_element_type=jnp.float32,
    )
    return lax.psum_scatter(
        partial_value.astype(jnp.bfloat16), "head", scatter_dimension=1, tiled=True
    )


def solution(mesh):
    in_specs = (
        P(("seq", "head"), None),
        P(("seq", "head"), None),
        P(("seq", "head"), None),
        P(None, "seq", None),
        P("head", "seq"),
    )
    out_specs = P("seq", "head")
    return jax.shard_map(body, mesh=mesh, in_specs=in_specs, out_specs=out_specs, check_vma=False)
```

```python
import jax
import jax.numpy as jnp
from jax import lax
from jax.experimental import pallas as pl
from jax.sharding import PartitionSpec as P

HEADS = 32
HD = 128
CLUSTERS = 128


def slot_table(block_ids, slot_depth):
    sub_rows = block_ids.shape[-1]
    onehot = (block_ids[..., None] == jnp.arange(CLUSTERS, dtype=jnp.int32)).astype(jnp.float32)
    lower = (jnp.arange(sub_rows)[:, None] >= jnp.arange(sub_rows)[None, :]).astype(jnp.float32)
    running = jnp.einsum("ts,abse->abte", lower, onehot)
    ranking = (jnp.sum(running * onehot, axis=-1) - 1.0).astype(jnp.int32)
    depth_hit = (ranking[..., None] == jnp.arange(slot_depth, dtype=jnp.int32)).astype(jnp.bfloat16)
    return onehot.astype(jnp.bfloat16)[..., :, None] * depth_hit[..., None, :]


def attend_kernel(q_ref, k_ref, v_ref, mask_ref, out_ref):
    for item in range(q_ref.shape[1]):
        scores = lax.dot_general(
            q_ref[0, item], k_ref[0, item], (((1,), (1,)), ((), ())),
            preferred_element_type=jnp.float32,
        ) * HD ** (-0.5)
        scores = jnp.where(mask_ref[item] > 0, scores, -1e30)
        row_max = jnp.max(scores, axis=-1, keepdims=True)
        raised = jnp.exp(scores - row_max)
        weights = (raised / jnp.sum(raised, axis=-1, keepdims=True)).astype(jnp.bfloat16)
        result = jnp.dot(weights, v_ref[0, item], preferred_element_type=jnp.float32)
        out_ref[:, item] = result.reshape(out_ref.shape[0], out_ref.shape[2], HD).astype(out_ref.dtype)


def attend_blocks(packed, validity, n_dest):
    items, slots, _ = packed.shape[1:]
    lanes = slots // n_dest
    mask = validity.astype(jnp.float32).reshape(items, 1, slots)
    step = 4
    specs = [pl.BlockSpec((1, step, slots, HD), lambda i, x=x: (x, i, 0, 0)) for x in range(3)]
    return pl.pallas_call(
        attend_kernel,
        grid=(items // step,),
        in_specs=specs + [pl.BlockSpec((step, 1, slots), lambda i: (i, 0, 0))],
        out_specs=pl.BlockSpec((n_dest, step, lanes, HD), lambda i: (0, i, 0, 0)),
        out_shape=jax.ShapeDtypeStruct((n_dest, items, lanes, HD), jnp.bfloat16),
        cost_estimate=pl.CostEstimate(
            flops=40 * items * slots * slots * HD,
            transcendentals=10 * items * slots * slots,
            bytes_accessed=4 * items * slots * HD * 2,
        ),
    )(packed, packed, packed, mask)


def body(queries, keys, values, cluster_ids, out_weight):
    n_seq = lax.axis_size("seq")
    n_head = lax.axis_size("head")
    head_group = lax.axis_index("head")
    tok_dev = cluster_ids.shape[1]
    sub_rows = tok_dev // n_head
    group_heads = HEADS // n_head
    slot_depth = max(2, 2 * tok_dev // (n_head * CLUSTERS))
    per_owner = group_heads * CLUSTERS // n_seq
    n_src = n_seq * n_head
    all_ids = cluster_ids[:, :, 0]

    own_ids = lax.dynamic_slice_in_dim(all_ids, head_group * sub_rows, sub_rows, 1)
    own_table = slot_table(own_ids[:, None, :], slot_depth)[:, 0]
    stacked = jnp.stack([t.reshape(sub_rows, HEADS, HD) for t in (queries, keys, values)])
    packed = jnp.einsum(
        "htcr,xthd->xhcrd", own_table, stacked, preferred_element_type=jnp.float32
    ).astype(jnp.bfloat16)
    packed = packed.reshape(3, n_head, per_owner, n_seq, slot_depth, HD)
    packed = packed.transpose(0, 3, 1, 2, 4, 5).reshape(3, n_src, per_owner, slot_depth, HD)

    group_ids = lax.dynamic_slice_in_dim(cluster_ids, head_group * group_heads, group_heads, 0)
    arrived = lax.all_to_all(packed, ("seq", "head"), split_axis=1, concat_axis=1, tiled=True)
    arrived = arrived.transpose(0, 2, 1, 3, 4).reshape(3, per_owner, n_src * slot_depth, HD)

    seen_ids = lax.all_gather(group_ids, "seq", axis=1, tiled=True)
    seen_ids = seen_ids.reshape(group_heads, n_src, sub_rows)
    group_ids = group_ids[:, :, 0]
    owned = jnp.arange(CLUSTERS // n_seq, dtype=jnp.int32) * n_seq + lax.axis_index("seq")
    counts = jnp.sum(
        (seen_ids[:, None, :, :] == owned[None, :, None, None]).astype(jnp.int32), axis=-1
    )
    counts = counts.reshape(per_owner, n_src)
    valid = counts[:, :, None] > jnp.arange(slot_depth, dtype=jnp.int32)
    valid = valid.reshape(per_owner, n_src * slot_depth)
    result_block = attend_blocks(arrived, valid, n_seq)
    returned = lax.all_to_all(result_block, "seq", split_axis=0, concat_axis=0, tiled=True)
    returned = returned.transpose(1, 0, 2, 3).reshape(group_heads, CLUSTERS, n_head, slot_depth, HD)

    group_ids = group_ids.reshape(group_heads, n_head, sub_rows)
    home_table = slot_table(group_ids, slot_depth)
    gathered = jnp.einsum(
        "hltcr,hclrd->lthd", home_table, returned, preferred_element_type=jnp.float32
    ).astype(jnp.bfloat16)
    gathered = gathered.reshape(tok_dev, group_heads * HD)
    partial_value = jnp.dot(
        gathered,
        lax.all_gather(out_weight, "seq", axis=1, tiled=True),
        preferred_element_type=jnp.float32,
    )
    return lax.psum_scatter(
        partial_value.astype(jnp.bfloat16), "head", scatter_dimension=1, tiled=True
    )


def solution(mesh):
    in_specs = (
        P(("seq", "head"), None),
        P(("seq", "head"), None),
        P(("seq", "head"), None),
        P(None, "seq", None),
        P("head", "seq"),
    )
    out_specs = P("seq", "head")
    return jax.shard_map(body, mesh=mesh, in_specs=in_specs, out_specs=out_specs, check_vma=False)
```
